256 devices in a mesh: orb: 64 (over z, x, y_hi), grp: 4 (over y_lo, core).
Axes of the slice: x: 4, y: 4 (y_hi: 2, y_lo: 2; y = y_hi * 2 + y_lo), z: 8, core: 2. Of those that a mesh axis runs over, the one named last changes fastest.
Arguments:
- orbitals: bfloat16 [512, 64, 4096], P(('orb', 'grp')), may hold values from -6 to 6
- offsets: int32 [512, 3], replicated, may hold values from 0 to 15
- send_slot: int32 [4, 256], replicated, may hold values from 0 to 1
- pair_mask: int32 [4, 512], P(None, ('orb', 'grp')), may hold values from 0 to 1
Outputs:
- exchange_action: float32 [512, 64, 4096], P(('orb', 'grp'))
The draws below stay inside these ranges and needn't reach their ends.
All inputs are finite; a program needn't handle non-finite values.
Results may differ from the reference program's by a relative error of at most 0.0016.
Values may be sent and summed in bfloat16 or wider, within the bound.
No kernel may reach another device: no remote copies, remote signals or barrier semaphores. Data moves between devices by JAX's collectives and lax.ppermute only.
A program may use at most 128 MiB of HBM per device.

```python
import math
import jax
import jax.numpy as jnp
from jax import lax

L = 64
ORB_DEV = 2
ROUNDS = 4
SHIFT = 16
OWNERS = 256
ORBS = 512
FAR = 132


def draw_pair_mask(key, part):
    owner_total = ORBS // ORB_DEV
    key_level, key_pick, key_roll = jax.random.split(key, 3)
    levels = jax.random.randint(key_level, (owner_total,), 1, 5)
    picks = jax.random.permutation(key_pick, owner_total)
    levels = levels.at[picks[0]].set(4)
    levels = levels.at[picks[1]].set(1)
    orbital_levels = jnp.repeat(levels, ORB_DEV)
    rolls = jax.random.randint(key_roll, (ROUNDS, ORBS), 0, 4)
    return (rolls < orbital_levels[None, :]).astype(jnp.int32)


def place_ends(drawn, own_key, low, high):
    longest = drawn.shape.index(max(drawn.shape))
    spots = []
    for shift in (0, 1):
        where = [jax.random.randint(jax.random.fold_in(own_key, axis), (), 0, length) for axis, length in enumerate(drawn.shape)]
        where[longest] = (where[longest] + shift) % drawn.shape[longest]
        spots.append(tuple(where))
    return drawn.at[spots[0]].set(low).at[spots[1]].set(high)


def block_scale(own_key, dims, cuts, smallest, largest):
    level, own = 1.0, jax.random.fold_in(own_key, 6)
    for axis_at, parts in cuts:
        draws = jnp.exp(jax.random.uniform(jax.random.fold_in(own, axis_at), (parts,), jnp.float32, smallest / len(cuts), largest / len(cuts)))
        level = level * jnp.repeat(draws, dims[axis_at] // parts).reshape([-1 if axis == axis_at else 1 for axis in range(len(dims))])
    return level


def centred(stream_key, extent, spread, most, cuts=(), held_as=jnp.bfloat16):
    drawn = spread * jax.random.normal(stream_key, extent, jnp.float32)
    if cuts:
        drawn = drawn * block_scale(stream_key, extent, cuts, -0.22, 0.18)
    return jnp.clip(drawn, -most, most).astype(held_as)


def setup_inputs(seed: int = 0) -> dict:
    seeds = jax.random.split(jax.random.key(seed), 5)
    orbitals = centred(seeds[0], (ORBS, L, L * L), 1.0, 6.0, ((0, 256),))
    offsets = place_ends(jax.random.randint(seeds[1], (ORBS, 3), 0, SHIFT), jax.random.fold_in(seeds[1], 1), 0, SHIFT - 1).astype(jnp.int32)
    send_slot = place_ends(jax.random.randint(seeds[2], (ROUNDS, OWNERS), 0, ORB_DEV), jax.random.fold_in(seeds[2], 1), 0, ORB_DEV - 1).astype(jnp.int32)
    pair_mask = draw_pair_mask(jax.random.fold_in(seeds[4], 71), 0)
    return {"orbitals": orbitals, "offsets": offsets, "send_slot": send_slot, "pair_mask": pair_mask}


screening = 0.005

def sine_table(box_size):
    indices = jnp.arange(box_size, dtype=jnp.float32) + 1.0
    scaling = math.sqrt(2.0 / (box_size + 1))
    sine_matrix = scaling * jnp.sin(math.pi * jnp.outer(indices, indices) / (box_size + 1))
    eigenvalues = 2.0 - 2.0 * jnp.cos(math.pi * indices / (box_size + 1))
    return (sine_matrix, eigenvalues)

def spectral_cube(eigenvalues):
    summed = eigenvalues[:, None, None] + eigenvalues[None, :, None] + eigenvalues[None, None, :]
    return 1.0 / (summed + screening)

def shift_cube(volume, offset_move, pad_reach):
    padded = jnp.pad(volume, pad_reach)
    starts = (offset_move + pad_reach).astype(jnp.int32)
    return lax.dynamic_slice(padded, (starts[0], starts[1], starts[2]), volume.shape)

def sine_three(field, sine_matrix):
    precise = lax.Precision.HIGHEST
    field = jnp.einsum('ia,ijk->ajk', sine_matrix, field, precision=precise)
    field = jnp.einsum('jb,ajk->abk', sine_matrix, field, precision=precise)
    return jnp.einsum('kc,abk->abc', sine_matrix, field, precision=precise)

def poisson(density, sine_matrix, spectral):
    return sine_three(sine_three(density, sine_matrix) * spectral, sine_matrix)

def reference(orbitals, offsets, send_slot, pair_mask):
    owner_count = ORBS // ORB_DEV
    cubes = orbitals.reshape(ORBS, L, L, L)
    sine_matrix, eigenvalues = sine_table(L)
    spectral = spectral_cube(eigenvalues)
    totals = jnp.zeros((ORBS, L, L, L), jnp.float32)
    for round_index in range(ROUNDS):
        magnitude = 1 if round_index // 2 % 2 == 0 else FAR
        stride = magnitude if round_index % 2 == 0 else -magnitude

        def receive(owner_index):
            sender = (owner_index - stride) % owner_count
            sent_index = (sender * ORB_DEV + send_slot[round_index, sender]).astype(jnp.int32)
            source_box = cubes[sent_index].astype(jnp.float32)
            local_terms = []
            return_box = jnp.zeros((L, L, L), jnp.float32)
            for member in range(ORB_DEV):
                orbital_index = (owner_index * ORB_DEV + member).astype(jnp.int32)
                offset_move = offsets[orbital_index] - offsets[sent_index]
                moved_box = shift_cube(source_box, offset_move, SHIFT)
                own_box = cubes[orbital_index].astype(jnp.float32)
                potential = poisson(own_box * moved_box, sine_matrix, spectral)
                weight = pair_mask[round_index, orbital_index].astype(jnp.float32)
                local_terms.append(weight * potential * moved_box)
                return_box = return_box + weight * shift_cube(potential * own_box, -offset_move, SHIFT)
            return (jnp.stack(local_terms), return_box.astype(jnp.bfloat16))
        local_all, back_all = lax.map(receive, jnp.arange(owner_count, dtype=jnp.int32))
        totals = totals + local_all.reshape(ORBS, L, L, L)
        receivers = jnp.arange(owner_count, dtype=jnp.int32)
        senders = (receivers - stride) % owner_count
        sent_all = (senders * ORB_DEV + send_slot[round_index, senders]).astype(jnp.int32)
        totals = totals.at[sent_all].add(back_all.astype(jnp.float32))
    return totals.reshape(ORBS, L, L * L)
```

```python
import math

import jax
import jax.numpy as jnp
from jax import lax
from jax.sharding import PartitionSpec as P


ROUNDS = 4


screening = 0.005


def shifted(value, axis, steps):
    count = lax.axis_size(axis)
    pairs = [(source, (source + steps) % count) for source in range(count)]
    return lax.ppermute(value, axis, pairs)


def sine_table(box_size):
    indices = jnp.arange(box_size, dtype=jnp.float32) + 1.0
    scaling = math.sqrt(2.0 / (box_size + 1))
    sine_matrix = scaling * jnp.sin(math.pi * jnp.outer(indices, indices) / (box_size + 1))
    eigenvalues = 2.0 - 2.0 * jnp.cos(math.pi * indices / (box_size + 1))
    return (sine_matrix, eigenvalues)


def pick(table, index):
    hit = jnp.arange(table.shape[0], dtype=jnp.int32) == index
    hit = hit.reshape((table.shape[0],) + (1,) * (table.ndim - 1))
    return jnp.sum(jnp.where(hit, table, jnp.zeros_like(table)), axis=0)


def shift_mats(moves, box_size, dtype):
    rows = jnp.arange(box_size, dtype=jnp.int32)[:, None]
    cols = jnp.arange(box_size, dtype=jnp.int32)[None, :]
    hit = cols[None, None] == rows[None, None] + moves[:, :, None, None]
    return hit.astype(dtype)


def shift_boxes(boxes, mats, precise, out_dtype):
    f = jnp.einsum("nai,nijk->najk", mats[:, 0], boxes, precision=precise,
                   preferred_element_type=jnp.float32).astype(out_dtype)
    f = jnp.einsum("nbj,najk->nabk", mats[:, 1], f, precision=precise,
                   preferred_element_type=jnp.float32).astype(out_dtype)
    f = jnp.einsum("nck,nabk->nabc", mats[:, 2], f, precision=precise,
                   preferred_element_type=jnp.float32).astype(out_dtype)
    return f


def sine_three(field, sine_matrix):
    precise = lax.Precision.HIGH
    field = jnp.einsum("ia,nijk->najk", sine_matrix, field, precision=precise,
                       preferred_element_type=jnp.float32)
    field = jnp.einsum("jb,najk->nabk", sine_matrix, field, precision=precise,
                       preferred_element_type=jnp.float32)
    return jnp.einsum("kc,nabk->nabc", sine_matrix, field, precision=precise,
                      preferred_element_type=jnp.float32)


def layer(orbitals, offsets, send_slot, pair_mask):
    owner_count = lax.axis_size(("orb", "grp"))
    far_stride = lax.axis_size("grp") * (lax.axis_size("orb") // 2 + 1)
    owner_index = lax.axis_index(("orb", "grp"))
    local_count = orbitals.shape[0]
    box_size = orbitals.shape[1]
    sine_matrix, eigenvalues = sine_table(box_size)
    summed = eigenvalues[:, None, None] + eigenvalues[None, :, None] + eigenvalues[None, None, :]
    spectral = 1.0 / (summed + screening)
    cubes = orbitals.reshape(local_count, box_size, box_size, box_size)
    own_f32 = cubes.astype(jnp.float32)
    members = jnp.arange(local_count, dtype=jnp.int32)
    own_offsets = jnp.stack(
        [pick(offsets, owner_index * local_count + m) for m in range(local_count)]
    )
    strides = []
    for round_index in range(ROUNDS):
        magnitude = 1 if round_index // 2 % 2 == 0 else far_stride
        strides.append(magnitude if round_index % 2 == 0 else -magnitude)
    arrived = []
    my_slots = []
    for round_index in range(ROUNDS):
        slot_mine = pick(send_slot[round_index], owner_index)
        my_slots.append(slot_mine)
        outgoing = pick(orbitals, slot_mine)
        arrived.append(shifted(outgoing, ("orb", "grp"), strides[round_index] % owner_count))
    totals = jnp.zeros((local_count, box_size, box_size, box_size), jnp.float32)
    returned = []
    for round_index in range(ROUNDS):
        received = arrived[round_index].reshape(box_size, box_size, box_size)
        sender = (owner_index - strides[round_index]) % owner_count
        sent_index = sender * local_count + pick(send_slot[round_index], sender)
        sent_offset = pick(offsets, sent_index)
        moves = own_offsets - sent_offset[None, :]
        weights = pair_mask[round_index].astype(jnp.float32)[:, None, None, None]
        fwd_mats = shift_mats(moves, box_size, jnp.bfloat16)
        back_mats = shift_mats(-moves, box_size, jnp.float32)
        moved = shift_boxes(
            jnp.broadcast_to(received[None], (local_count,) + received.shape),
            fwd_mats, lax.Precision.DEFAULT, jnp.bfloat16,
        ).astype(jnp.float32)
        density = own_f32 * moved
        potential = sine_three(sine_three(density, sine_matrix) * spectral, sine_matrix)
        weighted = weights * potential
        totals = totals + weighted * moved
        product = weighted * own_f32
        back = shift_boxes(product, back_mats, lax.Precision.HIGHEST, jnp.float32)
        back = jnp.sum(back, axis=0).astype(jnp.bfloat16)
        if round_index + 1 < ROUNDS:
            back, arrived[round_index + 1], totals = lax.optimization_barrier(
                (back, arrived[round_index + 1], totals)
            )
        returned.append(
            shifted(back, ("orb", "grp"), -strides[round_index] % owner_count)
        )
    for round_index in range(ROUNDS):
        hit = (members == my_slots[round_index])[:, None, None, None]
        totals = totals + jnp.where(
            hit, returned[round_index].astype(jnp.float32)[None], 0.0
        )
    return totals.reshape(local_count, box_size, box_size * box_size)


def solution(mesh):
    in_specs = (P(("orb", "grp"), None, None), P(), P(), P(None, ("orb", "grp")))
    out_specs = P(("orb", "grp"), None, None)
    return jax.shard_map(layer, mesh=mesh, in_specs=in_specs, out_specs=out_specs, check_vma=False)
```

```python
import math

import jax
import jax.numpy as jnp
from jax import lax
from jax.sharding import PartitionSpec as P


ROUNDS = 4


screening = 0.005


def shifted(value, axis, steps):
    count = lax.axis_size(axis)
    pairs = [(source, (source + steps) % count) for source in range(count)]
    return lax.ppermute(value, axis, pairs)


def sine_table(box_size):
    indices = jnp.arange(box_size, dtype=jnp.float32) + 1.0
    scaling = math.sqrt(2.0 / (box_size + 1))
    sine_matrix = scaling * jnp.sin(math.pi * jnp.outer(indices, indices) / (box_size + 1))
    eigenvalues = 2.0 - 2.0 * jnp.cos(math.pi * indices / (box_size + 1))
    return (sine_matrix, eigenvalues)


ORDER = (0, 2, 3, 1)


def pick(table, index):
    hit = jnp.arange(table.shape[0], dtype=jnp.int32) == index
    hit = hit.reshape((table.shape[0],) + (1,) * (table.ndim - 1))
    return jnp.sum(jnp.where(hit, table, jnp.zeros_like(table)), axis=0)


def shift_box(source_box, offset_move, box_size, pad_reach):
    pad_cols = pad_reach * box_size + pad_reach
    padded = jnp.pad(source_box, ((pad_reach, pad_reach), (pad_cols, pad_cols)))
    row_start = pad_reach + offset_move[0]
    col_start = pad_cols + offset_move[1] * box_size + offset_move[2]
    moved_box = lax.dynamic_slice(padded, (row_start, col_start), (box_size, box_size * box_size))
    depth_index = jnp.arange(box_size * box_size, dtype=jnp.int32) % box_size + offset_move[2]
    inside = (depth_index >= 0) & (depth_index < box_size)
    return jnp.where(inside[None, :], moved_box, jnp.zeros_like(moved_box))


def solve_couple(density, sine_matrix, depth_block, spectral):
    box_size = sine_matrix.shape[0]
    couple_width = 2 * box_size
    precise = lax.Precision.HIGHEST
    lead_dims = (((0,), (0,)), ((), ()))
    middle_dims = (((0,), (1,)), ((), ()))
    field = jnp.dot(
        density.reshape(box_size * box_size, couple_width),
        depth_block,
        precision=precise,
        preferred_element_type=jnp.float32,
    )
    field = field.reshape(box_size, box_size, couple_width)
    field = lax.dot_general(
        sine_matrix, field, lead_dims, precision=precise, preferred_element_type=jnp.float32
    )
    field = lax.dot_general(
        sine_matrix, field, middle_dims, precision=precise, preferred_element_type=jnp.float32
    )
    field = field * spectral
    field = lax.dot_general(
        sine_matrix, field, lead_dims, precision=precise, preferred_element_type=jnp.float32
    )
    field = lax.dot_general(
        sine_matrix, field, middle_dims, precision=precise, preferred_element_type=jnp.float32
    )
    field = jnp.dot(
        field.reshape(box_size * box_size, couple_width),
        depth_block,
        precision=precise,
        preferred_element_type=jnp.float32,
    )
    return field.reshape(box_size, box_size, couple_width)


def to_couple(first_box, second_box, box_size):
    return jnp.concatenate(
        (
            first_box.reshape(box_size, box_size, box_size),
            second_box.reshape(box_size, box_size, box_size),
        ),
        axis=2,
    )


def from_couple(couple, member, box_size):
    return couple[:, :, member * box_size : (member + 1) * box_size].reshape(
        box_size, box_size * box_size
    )


def layer(orbitals, offsets, send_slot, pair_mask):
    owner_count = lax.axis_size(("orb", "grp"))
    far_stride = lax.axis_size("grp") * (lax.axis_size("orb") // 2 + 1)
    owner_index = lax.axis_index(("orb", "grp"))
    local_count = orbitals.shape[0]
    box_size = orbitals.shape[1]
    pad_reach = box_size // 4
    sine_matrix, eigenvalues = sine_table(box_size)
    depth_block = jnp.kron(jnp.eye(2, dtype=jnp.float32), sine_matrix)
    summed = eigenvalues[:, None, None] + eigenvalues[None, :, None] + eigenvalues[None, None, :]
    spectral_part = 1.0 / (summed + screening)
    spectral = jnp.concatenate((spectral_part, spectral_part), axis=2)
    members = jnp.arange(local_count, dtype=jnp.int32)
    own_offsets = jnp.stack(
        [pick(offsets, owner_index * local_count + m) for m in range(local_count)]
    )
    strides = []
    for round_index in range(ROUNDS):
        magnitude = 1 if round_index // 2 % 2 == 0 else far_stride
        strides.append(magnitude if round_index % 2 == 0 else -magnitude)
    my_slots = [pick(send_slot[r], owner_index) for r in range(ROUNDS)]
    sent_offsets = []
    for round_index in range(ROUNDS):
        sender = (owner_index - strides[round_index]) % owner_count
        sent_index = sender * local_count + pick(send_slot[round_index], sender)
        sent_offsets.append(pick(offsets, sent_index))
    move_table = own_offsets[None, :, :] - jnp.stack(sent_offsets)[:, None, :]
    empty_box = jnp.zeros((box_size, box_size * box_size), jnp.float32)
    totals = jnp.zeros((local_count, box_size, box_size * box_size), jnp.float32)
    arrived = {}
    for round_index in range(ROUNDS):
        outgoing = pick(orbitals, my_slots[round_index])
        arrived[round_index] = shifted(
            outgoing, ("orb", "grp"), strides[round_index] % owner_count
        )
    returned = {}
    for position, round_index in enumerate(ORDER):
        received = arrived[round_index]
        moves = []
        moved_boxes = []
        owned_boxes = []
        weights = []
        for member in range(local_count):
            offset_move = move_table[round_index, member]
            moves.append(offset_move)
            moved_boxes.append(
                shift_box(received, offset_move, box_size, pad_reach).astype(jnp.float32)
            )
            owned_boxes.append(orbitals[member].astype(jnp.float32))
            weights.append(pair_mask[round_index, member].astype(jnp.float32))
        density = to_couple(
            owned_boxes[0] * moved_boxes[0], owned_boxes[1] * moved_boxes[1], box_size
        )
        potential = solve_couple(density, sine_matrix, depth_block, spectral)
        gathered = empty_box
        for position_m in range(2):
            member_potential = from_couple(potential, position_m, box_size)
            term = weights[position_m] * member_potential * moved_boxes[position_m]
            hit = members == position_m
            totals = totals + jnp.where(hit[:, None, None], term[None], 0.0)
            product = weights[position_m] * member_potential * owned_boxes[position_m]
            gathered = gathered + shift_box(product, -moves[position_m], box_size, pad_reach)
        back = gathered.astype(jnp.bfloat16)
        if position + 1 < ROUNDS:
            nxt = ORDER[position + 1]
            back, arrived[nxt], totals = lax.optimization_barrier(
                (back, arrived[nxt], totals)
            )
        returned[round_index] = shifted(back, ("orb", "grp"), -strides[round_index] % owner_count)
    for round_index in range(ROUNDS):
        hit = (members == my_slots[round_index])[:, None, None]
        totals = totals + jnp.where(
            hit, returned[round_index].astype(jnp.float32)[None], 0.0
        )
    return totals


def solution(mesh):
    in_specs = (P(("orb", "grp"), None, None), P(), P(), P(None, ("orb", "grp")))
    out_specs = P(("orb", "grp"), None, None)
    return jax.shard_map(layer, mesh=mesh, in_specs=in_specs, out_specs=out_specs, check_vma=False)
```

```python
import math

import jax
import jax.numpy as jnp
from jax import lax
from jax.experimental import pallas as pl
from jax.experimental.pallas import tpu as pltpu
from jax.sharding import PartitionSpec as P


ROUNDS = 4


screening = 0.005


def shifted(value, axis, steps):
    count = lax.axis_size(axis)
    pairs = [(source, (source + steps) % count) for source in range(count)]
    return lax.ppermute(value, axis, pairs)


def sine_table(box_size):
    indices = jnp.arange(box_size, dtype=jnp.float32) + 1.0
    scaling = math.sqrt(2.0 / (box_size + 1))
    sine_matrix = scaling * jnp.sin(math.pi * jnp.outer(indices, indices) / (box_size + 1))
    eigenvalues = 2.0 - 2.0 * jnp.cos(math.pi * indices / (box_size + 1))
    return (sine_matrix, eigenvalues)


ORDER = (0, 2, 3, 1)


def _shift_one(x, wx, wy, wz):
    rows, lanes = x.shape
    s = wy * rows + wz
    r = pltpu.roll(x, (lanes - s) % lanes, 1)
    lane = lax.broadcasted_iota(jnp.int32, (1, lanes), 1)
    zz = lane % rows + wz
    yy = lane // rows + wy
    ok = (zz >= 0) & (zz < rows) & (yy >= 0) & (yy < rows)
    r = pltpu.roll(r, (rows - wx) % rows, 0)
    row = lax.broadcasted_iota(jnp.int32, (rows, 1), 0) + wx
    ok = ok & (row >= 0) & (row < rows)
    return jnp.where(ok, r, 0.0)


def _fwd_kernel(moves_ref, recv_ref, moved_ref):
    x = recv_ref[...].astype(jnp.float32)
    for m in range(moved_ref.shape[0]):
        moved_ref[m] = _shift_one(x, moves_ref[3 * m], moves_ref[3 * m + 1], moves_ref[3 * m + 2])


def _back_kernel(moves_ref, prod_ref, out_ref):
    acc = None
    for m in range(prod_ref.shape[0]):
        part = _shift_one(prod_ref[m], -moves_ref[3 * m], -moves_ref[3 * m + 1], -moves_ref[3 * m + 2])
        acc = part if acc is None else acc + part
    out_ref[...] = acc.astype(out_ref.dtype)


def shift_forward(received, moves, count):
    rows, lanes = received.shape
    return pl.pallas_call(
        _fwd_kernel,
        out_shape=jax.ShapeDtypeStruct((count, rows, lanes), jnp.float32),
        in_specs=[pl.BlockSpec(memory_space=pltpu.SMEM), pl.BlockSpec(memory_space=pltpu.VMEM)],
        out_specs=pl.BlockSpec(memory_space=pltpu.VMEM),
    )(moves.reshape(-1), received)


def shift_back(products, moves):
    _, rows, lanes = products.shape
    return pl.pallas_call(
        _back_kernel,
        out_shape=jax.ShapeDtypeStruct((rows, lanes), jnp.bfloat16),
        in_specs=[pl.BlockSpec(memory_space=pltpu.SMEM), pl.BlockSpec(memory_space=pltpu.VMEM)],
        out_specs=pl.BlockSpec(memory_space=pltpu.VMEM),
    )(moves.reshape(-1), products)


def pick(table, index):
    hit = jnp.arange(table.shape[0], dtype=jnp.int32) == index
    hit = hit.reshape((table.shape[0],) + (1,) * (table.ndim - 1))
    return jnp.sum(jnp.where(hit, table, jnp.zeros_like(table)), axis=0)


def solve_couple(density, sine_matrix, depth_block, spectral):
    box_size = sine_matrix.shape[0]
    couple_width = 2 * box_size
    precise = lax.Precision.HIGH
    lead_dims = (((0,), (0,)), ((), ()))
    middle_dims = (((0,), (1,)), ((), ()))
    field = jnp.dot(
        density.reshape(box_size * box_size, couple_width),
        depth_block,
        precision=precise,
        preferred_element_type=jnp.float32,
    )
    field = field.reshape(box_size, box_size, couple_width)
    field = lax.dot_general(
        sine_matrix, field, lead_dims, precision=precise, preferred_element_type=jnp.float32
    )
    field = lax.dot_general(
        sine_matrix, field, middle_dims, precision=precise, preferred_element_type=jnp.float32
    )
    field = field * spectral
    field = lax.dot_general(
        sine_matrix, field, lead_dims, precision=precise, preferred_element_type=jnp.float32
    )
    field = lax.dot_general(
        sine_matrix, field, middle_dims, precision=precise, preferred_element_type=jnp.float32
    )
    field = jnp.dot(
        field.reshape(box_size * box_size, couple_width),
        depth_block,
        precision=precise,
        preferred_element_type=jnp.float32,
    )
    return field.reshape(box_size, box_size, couple_width)


def to_couple(first_box, second_box, box_size):
    return jnp.concatenate(
        (
            first_box.reshape(box_size, box_size, box_size),
            second_box.reshape(box_size, box_size, box_size),
        ),
        axis=2,
    )


def from_couple(couple, member, box_size):
    return couple[:, :, member * box_size : (member + 1) * box_size].reshape(
        box_size, box_size * box_size
    )


def layer(orbitals, offsets, send_slot, pair_mask):
    owner_count = lax.axis_size(("orb", "grp"))
    far_stride = lax.axis_size("grp") * (lax.axis_size("orb") // 2 + 1)
    owner_index = lax.axis_index(("orb", "grp"))
    local_count = orbitals.shape[0]
    box_size = orbitals.shape[1]
    sine_matrix, eigenvalues = sine_table(box_size)
    depth_block = jnp.kron(jnp.eye(2, dtype=jnp.float32), sine_matrix)
    summed = eigenvalues[:, None, None] + eigenvalues[None, :, None] + eigenvalues[None, None, :]
    spectral_part = 1.0 / (summed + screening)
    spectral = jnp.concatenate((spectral_part, spectral_part), axis=2)
    members = jnp.arange(local_count, dtype=jnp.int32)
    own_offsets = jnp.stack(
        [pick(offsets, owner_index * local_count + m) for m in range(local_count)]
    )
    strides = []
    for round_index in range(ROUNDS):
        magnitude = 1 if round_index // 2 % 2 == 0 else far_stride
        strides.append(magnitude if round_index % 2 == 0 else -magnitude)
    my_slots = [pick(send_slot[r], owner_index) for r in range(ROUNDS)]
    sent_offsets = []
    for round_index in range(ROUNDS):
        sender = (owner_index - strides[round_index]) % owner_count
        sent_index = sender * local_count + pick(send_slot[round_index], sender)
        sent_offsets.append(pick(offsets, sent_index))
    move_table = own_offsets[None, :, :] - jnp.stack(sent_offsets)[:, None, :]
    totals = jnp.zeros((local_count, box_size, box_size * box_size), jnp.float32)
    arrived = {}
    for round_index in range(ROUNDS):
        outgoing = pick(orbitals, my_slots[round_index])
        arrived[round_index] = shifted(
            outgoing, ("orb", "grp"), strides[round_index] % owner_count
        )
    returned = {}
    for position, round_index in enumerate(ORDER):
        received = arrived[round_index]
        round_moves = move_table[round_index]
        moved_stack = shift_forward(received, round_moves, local_count)
        moved_boxes = [moved_stack[m] for m in range(local_count)]
        owned_boxes = [orbitals[m].astype(jnp.float32) for m in range(local_count)]
        weights = [pair_mask[round_index, m].astype(jnp.float32) for m in range(local_count)]
        density = to_couple(
            owned_boxes[0] * moved_boxes[0], owned_boxes[1] * moved_boxes[1], box_size
        )
        potential = solve_couple(density, sine_matrix, depth_block, spectral)
        products = []
        for position_m in range(2):
            member_potential = from_couple(potential, position_m, box_size)
            term = weights[position_m] * member_potential * moved_boxes[position_m]
            hit = members == position_m
            totals = totals + jnp.where(hit[:, None, None], term[None], 0.0)
            products.append(weights[position_m] * member_potential * owned_boxes[position_m])
        back = shift_back(jnp.stack(products), round_moves)
        if position + 1 < ROUNDS:
            nxt = ORDER[position + 1]
            back, arrived[nxt], totals = lax.optimization_barrier(
                (back, arrived[nxt], totals)
            )
        returned[round_index] = shifted(back, ("orb", "grp"), -strides[round_index] % owner_count)
    for round_index in range(ROUNDS):
        hit = (members == my_slots[round_index])[:, None, None]
        totals = totals + jnp.where(
            hit, returned[round_index].astype(jnp.float32)[None], 0.0
        )
    return totals


def solution(mesh):
    in_specs = (P(("orb", "grp"), None, None), P(), P(), P(None, ("orb", "grp")))
    out_specs = P(("orb", "grp"), None, None)
    return jax.shard_map(layer, mesh=mesh, in_specs=in_specs, out_specs=out_specs, check_vma=False)
```

```python
import math

import jax
import jax.numpy as jnp
from jax import lax
from jax.experimental import pallas as pl
from jax.experimental.pallas import tpu as pltpu
from jax.sharding import PartitionSpec as P


ROUNDS = 4


screening = 0.005


def shifted(value, axis, steps):
    count = lax.axis_size(axis)
    pairs = [(source, (source + steps) % count) for source in range(count)]
    return lax.ppermute(value, axis, pairs)


def sine_table(box_size):
    indices = jnp.arange(box_size, dtype=jnp.float32) + 1.0
    scaling = math.sqrt(2.0 / (box_size + 1))
    sine_matrix = scaling * jnp.sin(math.pi * jnp.outer(indices, indices) / (box_size + 1))
    eigenvalues = 2.0 - 2.0 * jnp.cos(math.pi * indices / (box_size + 1))
    return (sine_matrix, eigenvalues)


ORDER = (0, 2, 3, 1)


def _shift_one(x, wx, wy, wz):
    rows, lanes = x.shape
    s = wy * rows + wz
    r = pltpu.roll(x, (lanes - s) % lanes, 1)
    lane = lax.broadcasted_iota(jnp.int32, (1, lanes), 1)
    zz = lane % rows + wz
    yy = lane // rows + wy
    ok = (zz >= 0) & (zz < rows) & (yy >= 0) & (yy < rows)
    r = pltpu.roll(r, (rows - wx) % rows, 0)
    row = lax.broadcasted_iota(jnp.int32, (rows, 1), 0) + wx
    ok = ok & (row >= 0) & (row < rows)
    return jnp.where(ok, r, 0.0)


def _join_chunk(first, second, half):
    even = jnp.where(half, first, pltpu.roll(second, 64, 1))
    odd = jnp.where(half, pltpu.roll(first, 64, 1), second)
    return even, odd


def _split_chunk(even, odd, half):
    first = jnp.where(half, even, pltpu.roll(odd, 64, 1))
    second = jnp.where(half, pltpu.roll(even, 64, 1), odd)
    return first, second


def _fwd_kernel(moves_ref, recv_ref, own_ref, dens_ref, work_ref):
    x = recv_ref[...].astype(jnp.float32)
    for m in range(own_ref.shape[0]):
        moved = _shift_one(x, moves_ref[3 * m], moves_ref[3 * m + 1], moves_ref[3 * m + 2])
        work_ref[m] = own_ref[m].astype(jnp.float32) * moved
    half = lax.broadcasted_iota(jnp.int32, (1, 128), 1) < 64

    def body(c, carry):
        cols = pl.ds(pl.multiple_of(c * 128, 128), 128)
        even, odd = _join_chunk(work_ref[0, :, cols], work_ref[1, :, cols], half)
        dens_ref[2 * c] = even
        dens_ref[2 * c + 1] = odd
        return carry

    lax.fori_loop(0, dens_ref.shape[0] // 2, body, 0)


def _back_kernel(meta_ref, recv_ref, own_ref, pot_ref, tot_in_ref, tot_ref, back_ref, work_ref):
    half = lax.broadcasted_iota(jnp.int32, (1, 128), 1) < 64

    def body(c, carry):
        cols = pl.ds(pl.multiple_of(c * 128, 128), 128)
        first, second = _split_chunk(pot_ref[2 * c], pot_ref[2 * c + 1], half)
        work_ref[0, :, cols] = first
        work_ref[1, :, cols] = second
        return carry

    lax.fori_loop(0, pot_ref.shape[0] // 2, body, 0)
    x = recv_ref[...].astype(jnp.float32)
    acc = None
    for m in range(own_ref.shape[0]):
        wx, wy, wz = meta_ref[3 * m], meta_ref[3 * m + 1], meta_ref[3 * m + 2]
        weight = meta_ref[6 + m].astype(jnp.float32)
        moved = _shift_one(x, wx, wy, wz)
        weighted = weight * work_ref[m]
        tot_ref[m] = tot_in_ref[m] + weighted * moved
        product = weighted * own_ref[m].astype(jnp.float32)
        part = _shift_one(product, -wx, -wy, -wz)
        acc = part if acc is None else acc + part
    back_ref[...] = acc.astype(back_ref.dtype)


def shift_density(received, own, moves):
    rows, _ = received.shape
    smem = pl.BlockSpec(memory_space=pltpu.SMEM)
    vmem = pl.BlockSpec(memory_space=pltpu.VMEM)
    return pl.pallas_call(
        _fwd_kernel,
        out_shape=jax.ShapeDtypeStruct((rows, rows, 2 * rows), jnp.float32),
        in_specs=[smem, vmem, vmem],
        out_specs=vmem,
        scratch_shapes=[pltpu.VMEM(own.shape, jnp.float32)],
    )(moves.reshape(-1), received, own)


def back_terms(received, own, potential, totals, meta):
    rows, lanes = received.shape
    smem = pl.BlockSpec(memory_space=pltpu.SMEM)
    vmem = pl.BlockSpec(memory_space=pltpu.VMEM)
    return pl.pallas_call(
        _back_kernel,
        out_shape=(
            jax.ShapeDtypeStruct(totals.shape, jnp.float32),
            jax.ShapeDtypeStruct((rows, lanes), jnp.bfloat16),
        ),
        in_specs=[smem, vmem, vmem, vmem, vmem],
        out_specs=(vmem, vmem),
        scratch_shapes=[pltpu.VMEM(own.shape, jnp.float32)],
        input_output_aliases={4: 0},
    )(meta, received, own, potential, totals)


def solve_swapped(density, sine_matrix, depth_block, spectral):
    box_size = sine_matrix.shape[0]
    precise = lax.Precision.HIGH

    def three(field):
        field = jnp.dot(
            field.reshape(box_size * box_size, 2 * box_size), depth_block,
            precision=precise, preferred_element_type=jnp.float32,
        ).reshape(box_size, box_size, 2 * box_size)
        field = jnp.einsum("ax,yxk->yak", sine_matrix, field, precision=precise,
                           preferred_element_type=jnp.float32)
        return jnp.einsum("by,yxk->bxk", sine_matrix, field, precision=precise,
                          preferred_element_type=jnp.float32)

    return three(three(density) * spectral)


def pick(table, index):
    hit = jnp.arange(table.shape[0], dtype=jnp.int32) == index
    hit = hit.reshape((table.shape[0],) + (1,) * (table.ndim - 1))
    return jnp.sum(jnp.where(hit, table, jnp.zeros_like(table)), axis=0)


def layer(orbitals, offsets, send_slot, pair_mask):
    owner_count = lax.axis_size(("orb", "grp"))
    far_stride = lax.axis_size("grp") * (lax.axis_size("orb") // 2 + 1)
    owner_index = lax.axis_index(("orb", "grp"))
    local_count = orbitals.shape[0]
    box_size = orbitals.shape[1]
    sine_matrix, eigenvalues = sine_table(box_size)
    depth_block = jnp.kron(jnp.eye(2, dtype=jnp.float32), sine_matrix)
    summed = eigenvalues[:, None, None] + eigenvalues[None, :, None] + eigenvalues[None, None, :]
    spectral_part = 1.0 / (summed + screening)
    spectral = jnp.concatenate((spectral_part, spectral_part), axis=2)
    members = jnp.arange(local_count, dtype=jnp.int32)
    own_offsets = jnp.stack(
        [pick(offsets, owner_index * local_count + m) for m in range(local_count)]
    )
    strides = []
    for round_index in range(ROUNDS):
        magnitude = 1 if round_index // 2 % 2 == 0 else far_stride
        strides.append(magnitude if round_index % 2 == 0 else -magnitude)
    my_slots = [pick(send_slot[r], owner_index) for r in range(ROUNDS)]
    sent_offsets = []
    for round_index in range(ROUNDS):
        sender = (owner_index - strides[round_index]) % owner_count
        sent_index = sender * local_count + pick(send_slot[round_index], sender)
        sent_offsets.append(pick(offsets, sent_index))
    move_table = own_offsets[None, :, :] - jnp.stack(sent_offsets)[:, None, :]
    totals = jnp.zeros((local_count, box_size, box_size * box_size), jnp.float32)
    arrived = {}
    for round_index in range(ROUNDS):
        outgoing = pick(orbitals, my_slots[round_index])
        arrived[round_index] = shifted(
            outgoing, ("orb", "grp"), strides[round_index] % owner_count
        )
    returned = {}
    for position, round_index in enumerate(ORDER):
        received = arrived[round_index]
        round_moves = move_table[round_index]
        density = shift_density(received, orbitals, round_moves)
        potential = solve_swapped(density, sine_matrix, depth_block, spectral)
        meta = jnp.concatenate((round_moves.reshape(-1), pair_mask[round_index]))
        totals, back = back_terms(received, orbitals, potential, totals, meta)
        if position + 1 < ROUNDS:
            nxt = ORDER[position + 1]
            back, arrived[nxt], totals = lax.optimization_barrier(
                (back, arrived[nxt], totals)
            )
        returned[round_index] = shifted(back, ("orb", "grp"), -strides[round_index] % owner_count)
    for round_index in range(ROUNDS):
        hit = (members == my_slots[round_index])[:, None, None]
        totals = totals + jnp.where(
            hit, returned[round_index].astype(jnp.float32)[None], 0.0
        )
    return totals


def solution(mesh):
    in_specs = (P(("orb", "grp"), None, None), P(), P(), P(None, ("orb", "grp")))
    out_specs = P(("orb", "grp"), None, None)
    return jax.shard_map(layer, mesh=mesh, in_specs=in_specs, out_specs=out_specs, check_vma=False)
```

```python
import math

import jax
import jax.numpy as jnp
from jax import lax
from jax.experimental import pallas as pl
from jax.experimental.pallas import tpu as pltpu
from jax.sharding import PartitionSpec as P


ROUNDS = 4


screening = 0.005


def shifted(value, axis, steps):
    count = lax.axis_size(axis)
    pairs = [(source, (source + steps) % count) for source in range(count)]
    return lax.ppermute(value, axis, pairs)


def sine_table(box_size):
    indices = jnp.arange(box_size, dtype=jnp.float32) + 1.0
    scaling = math.sqrt(2.0 / (box_size + 1))
    sine_matrix = scaling * jnp.sin(math.pi * jnp.outer(indices, indices) / (box_size + 1))
    eigenvalues = 2.0 - 2.0 * jnp.cos(math.pi * indices / (box_size + 1))
    return (sine_matrix, eigenvalues)


ORDER = (0, 2, 3, 1)


def _shift_one(x, wx, wy, wz):
    rows, lanes = x.shape
    s = wy * rows + wz
    r = pltpu.roll(x, (lanes - s) % lanes, 1)
    lane = lax.broadcasted_iota(jnp.int32, (1, lanes), 1)
    zz = lane % rows + wz
    yy = lane // rows + wy
    ok = (zz >= 0) & (zz < rows) & (yy >= 0) & (yy < rows)
    r = pltpu.roll(r, (rows - wx) % rows, 0)
    row = lax.broadcasted_iota(jnp.int32, (rows, 1), 0) + wx
    ok = ok & (row >= 0) & (row < rows)
    return jnp.where(ok, r, 0.0)


def _join_chunk(first, second, half):
    even = jnp.where(half, first, pltpu.roll(second, 64, 1))
    odd = jnp.where(half, pltpu.roll(first, 64, 1), second)
    return even, odd


def _split_chunk(even, odd, half):
    first = jnp.where(half, even, pltpu.roll(odd, 64, 1))
    second = jnp.where(half, pltpu.roll(even, 64, 1), odd)
    return first, second


def _fwd_kernel(moves_ref, recv_ref, own_ref, dens_ref, moved_ref, work_ref):
    x = recv_ref[...].astype(jnp.float32)
    for m in range(own_ref.shape[0]):
        moved = _shift_one(x, moves_ref[3 * m], moves_ref[3 * m + 1], moves_ref[3 * m + 2])
        moved_ref[m] = moved.astype(moved_ref.dtype)
        work_ref[m] = own_ref[m].astype(jnp.float32) * moved
    half = lax.broadcasted_iota(jnp.int32, (1, 128), 1) < 64

    def body(c, carry):
        cols = pl.ds(pl.multiple_of(c * 128, 128), 128)
        even, odd = _join_chunk(work_ref[0, :, cols], work_ref[1, :, cols], half)
        dens_ref[2 * c] = even
        dens_ref[2 * c + 1] = odd
        return carry

    lax.fori_loop(0, dens_ref.shape[0] // 2, body, 0)


def _back_kernel(meta_ref, moved_ref, own_ref, pot_ref, *rest):
    if len(rest) == 4:
        tot_in_ref, tot_ref, back_ref, work_ref = rest
    else:
        tot_in_ref = None
        tot_ref, back_ref, work_ref = rest
    half = lax.broadcasted_iota(jnp.int32, (1, 128), 1) < 64

    def body(c, carry):
        cols = pl.ds(pl.multiple_of(c * 128, 128), 128)
        first, second = _split_chunk(pot_ref[2 * c], pot_ref[2 * c + 1], half)
        work_ref[0, :, cols] = first
        work_ref[1, :, cols] = second
        return carry

    lax.fori_loop(0, pot_ref.shape[0] // 2, body, 0)
    acc = None
    for m in range(own_ref.shape[0]):
        wx, wy, wz = meta_ref[3 * m], meta_ref[3 * m + 1], meta_ref[3 * m + 2]
        weight = meta_ref[6 + m].astype(jnp.float32)
        weighted = weight * work_ref[m]
        term = weighted * moved_ref[m].astype(jnp.float32)
        tot_ref[m] = term if tot_in_ref is None else tot_in_ref[m] + term
        product = weighted * own_ref[m].astype(jnp.float32)
        part = _shift_one(product, -wx, -wy, -wz)
        acc = part if acc is None else acc + part
    back_ref[...] = acc.astype(back_ref.dtype)


def shift_density(received, own, moves):
    rows, _ = received.shape
    smem = pl.BlockSpec(memory_space=pltpu.SMEM)
    vmem = pl.BlockSpec(memory_space=pltpu.VMEM)
    return pl.pallas_call(
        _fwd_kernel,
        out_shape=(
            jax.ShapeDtypeStruct((rows, rows, 2 * rows), jnp.float32),
            jax.ShapeDtypeStruct(own.shape, jnp.bfloat16),
        ),
        in_specs=[smem, vmem, vmem],
        out_specs=(vmem, vmem),
        scratch_shapes=[pltpu.VMEM(own.shape, jnp.float32)],
    )(moves.reshape(-1), received, own)


def back_terms(moved, own, potential, totals, meta):
    _, rows, lanes = own.shape
    smem = pl.BlockSpec(memory_space=pltpu.SMEM)
    vmem = pl.BlockSpec(memory_space=pltpu.VMEM)
    operands = [meta, moved, own, potential]
    aliases = {}
    if totals is not None:
        operands.append(totals)
        aliases = {4: 0}
    return pl.pallas_call(
        _back_kernel,
        out_shape=(
            jax.ShapeDtypeStruct(own.shape, jnp.float32),
            jax.ShapeDtypeStruct((rows, lanes), jnp.bfloat16),
        ),
        in_specs=[smem] + [vmem] * (len(operands) - 1),
        out_specs=(vmem, vmem),
        scratch_shapes=[pltpu.VMEM(own.shape, jnp.float32)],
        input_output_aliases=aliases,
    )(*operands)


def solve_swapped(density, sine_matrix, depth_block, spectral):
    box_size = sine_matrix.shape[0]
    precise = lax.Precision.HIGH

    def along_z(field):
        return jnp.dot(
            field.reshape(box_size * box_size, 2 * box_size), depth_block,
            precision=precise, preferred_element_type=jnp.float32,
        ).reshape(box_size, box_size, 2 * box_size)

    def along_x(field):
        return jnp.einsum("ax,yxk->yak", sine_matrix, field, precision=precise,
                          preferred_element_type=jnp.float32)

    def along_y(field):
        return jnp.einsum("by,yxk->bxk", sine_matrix, field, precision=precise,
                          preferred_element_type=jnp.float32)

    field = along_y(along_x(along_z(density))) * spectral
    return along_z(along_x(along_y(field)))


def pick(table, index):
    hit = jnp.arange(table.shape[0], dtype=jnp.int32) == index
    hit = hit.reshape((table.shape[0],) + (1,) * (table.ndim - 1))
    return jnp.sum(jnp.where(hit, table, jnp.zeros_like(table)), axis=0)


def layer(orbitals, offsets, send_slot, pair_mask):
    owner_count = lax.axis_size(("orb", "grp"))
    far_stride = lax.axis_size("grp") * (lax.axis_size("orb") // 2 + 1)
    owner_index = lax.axis_index(("orb", "grp"))
    local_count = orbitals.shape[0]
    box_size = orbitals.shape[1]
    sine_matrix, eigenvalues = sine_table(box_size)
    depth_block = jnp.kron(jnp.eye(2, dtype=jnp.float32), sine_matrix)
    summed = eigenvalues[:, None, None] + eigenvalues[None, :, None] + eigenvalues[None, None, :]
    spectral_part = 1.0 / (summed + screening)
    spectral = jnp.concatenate((spectral_part, spectral_part), axis=2)
    members = jnp.arange(local_count, dtype=jnp.int32)
    own_offsets = jnp.stack(
        [pick(offsets, owner_index * local_count + m) for m in range(local_count)]
    )
    strides = []
    for round_index in range(ROUNDS):
        magnitude = 1 if round_index // 2 % 2 == 0 else far_stride
        strides.append(magnitude if round_index % 2 == 0 else -magnitude)
    my_slots = [pick(send_slot[r], owner_index) for r in range(ROUNDS)]
    sent_offsets = []
    for round_index in range(ROUNDS):
        sender = (owner_index - strides[round_index]) % owner_count
        sent_index = sender * local_count + pick(send_slot[round_index], sender)
        sent_offsets.append(pick(offsets, sent_index))
    move_table = own_offsets[None, :, :] - jnp.stack(sent_offsets)[:, None, :]
    totals = None
    arrived = {}
    for round_index in range(ROUNDS):
        outgoing = pick(orbitals, my_slots[round_index])
        arrived[round_index] = shifted(
            outgoing, ("orb", "grp"), strides[round_index] % owner_count
        )
    returned = {}
    for position, round_index in enumerate(ORDER):
        received = arrived[round_index]
        round_moves = move_table[round_index]
        density, moved = shift_density(received, orbitals, round_moves)
        potential = solve_swapped(density, sine_matrix, depth_block, spectral)
        meta = jnp.concatenate((round_moves.reshape(-1), pair_mask[round_index]))
        totals, back = back_terms(moved, orbitals, potential, totals, meta)
        if position + 1 < ROUNDS:
            nxt = ORDER[position + 1]
            back, arrived[nxt], totals = lax.optimization_barrier(
                (back, arrived[nxt], totals)
            )
        returned[round_index] = shifted(back, ("orb", "grp"), -strides[round_index] % owner_count)
    for round_index in range(ROUNDS):
        hit = (members == my_slots[round_index])[:, None, None]
        totals = totals + jnp.where(
            hit, returned[round_index].astype(jnp.float32)[None], 0.0
        )
    return totals


def solution(mesh):
    in_specs = (P(("orb", "grp"), None, None), P(), P(), P(None, ("orb", "grp")))
    out_specs = P(("orb", "grp"), None, None)
    return jax.shard_map(layer, mesh=mesh, in_specs=in_specs, out_specs=out_specs, check_vma=False)
```

```python
import math

import jax
import jax.numpy as jnp
from jax import lax
from jax.experimental import pallas as pl
from jax.experimental.pallas import tpu as pltpu
from jax.sharding import PartitionSpec as P


ROUNDS = 4


screening = 0.005


def shifted(value, axis, steps):
    count = lax.axis_size(axis)
    pairs = [(source, (source + steps) % count) for source in range(count)]
    return lax.ppermute(value, axis, pairs)


def sine_table(box_size):
    indices = jnp.arange(box_size, dtype=jnp.float32) + 1.0
    scaling = math.sqrt(2.0 / (box_size + 1))
    sine_matrix = scaling * jnp.sin(math.pi * jnp.outer(indices, indices) / (box_size + 1))
    eigenvalues = 2.0 - 2.0 * jnp.cos(math.pi * indices / (box_size + 1))
    return (sine_matrix, eigenvalues)


ORDER = (0, 2, 3, 1)

PADC = 9


def _chunk_cols(c):
    return pl.ds(pl.multiple_of(c * 128, 128), 128)


def _clear_pads(pad_ref):
    body = pad_ref.shape[0] - 2 * PADC
    zeros = jnp.zeros((PADC,) + pad_ref.shape[1:], jnp.float32)
    pad_ref[pl.ds(0, PADC)] = zeros
    pad_ref[pl.ds(PADC + body, PADC)] = zeros


def _shifted_chunk(pad_ref, j, wx, wy, wz):
    rows = pad_ref.shape[1]
    s = wy * rows + wz + 1024
    q = s // 128 - 8
    r = s % 128
    sh = (128 - r) % 128
    first = pltpu.roll(pad_ref[PADC + j + q], sh, 1)
    second = pltpu.roll(pad_ref[PADC + j + q + 1], sh, 1)
    lane = lax.broadcasted_iota(jnp.int32, (1, 128), 1)
    moved = jnp.where(lane < 128 - r, first, second)
    zz = lane % rows + wz
    yy = (j * 128 + lane) // rows + wy
    ok = (zz >= 0) & (zz < rows) & (yy >= 0) & (yy < rows)
    moved = pltpu.roll(moved, (rows - wx) % rows, 0)
    row = lax.broadcasted_iota(jnp.int32, (rows, 1), 0) + wx
    ok = ok & (row >= 0) & (row < rows)
    return jnp.where(ok, moved, 0.0)


def _join_chunk(first, second, half):
    even = jnp.where(half, first, pltpu.roll(second, 64, 1))
    odd = jnp.where(half, pltpu.roll(first, 64, 1), second)
    return even, odd


def _split_chunk(even, odd, half):
    first = jnp.where(half, even, pltpu.roll(odd, 64, 1))
    second = jnp.where(half, pltpu.roll(even, 64, 1), odd)
    return first, second


def _fwd_kernel(moves_ref, recv_ref, own_ref, dens_ref, moved_ref, work_ref, pad_ref):
    chunks = recv_ref.shape[1] // 128
    _clear_pads(pad_ref)

    def fill(c, carry):
        pad_ref[PADC + c] = recv_ref[:, _chunk_cols(c)].astype(jnp.float32)
        return carry

    lax.fori_loop(0, chunks, fill, 0)
    for m in range(own_ref.shape[0]):
        wx, wy, wz = moves_ref[3 * m], moves_ref[3 * m + 1], moves_ref[3 * m + 2]

        def shift(j, carry, m=m, wx=wx, wy=wy, wz=wz):
            cols = _chunk_cols(j)
            moved = _shifted_chunk(pad_ref, j, wx, wy, wz)
            moved_ref[m, :, cols] = moved.astype(moved_ref.dtype)
            work_ref[m, :, cols] = own_ref[m, :, cols].astype(jnp.float32) * moved
            return carry

        lax.fori_loop(0, chunks, shift, 0)
    half = lax.broadcasted_iota(jnp.int32, (1, 128), 1) < 64

    def body(c, carry):
        cols = _chunk_cols(c)
        even, odd = _join_chunk(work_ref[0, :, cols], work_ref[1, :, cols], half)
        dens_ref[2 * c] = even
        dens_ref[2 * c + 1] = odd
        return carry

    lax.fori_loop(0, dens_ref.shape[0] // 2, body, 0)


def _back_kernel(meta_ref, moved_ref, own_ref, pot_ref, *rest):
    if len(rest) == 5:
        tot_in_ref, tot_ref, back_ref, acc_ref, pad_ref = rest
    else:
        tot_in_ref = None
        tot_ref, back_ref, acc_ref, pad_ref = rest
    chunks = own_ref.shape[2] // 128
    half = lax.broadcasted_iota(jnp.int32, (1, 128), 1) < 64
    _clear_pads(pad_ref)
    count = own_ref.shape[0]
    for m in range(count):
        wx, wy, wz = meta_ref[3 * m], meta_ref[3 * m + 1], meta_ref[3 * m + 2]
        weight = meta_ref[6 + m].astype(jnp.float32)

        def terms(c, carry, m=m, weight=weight):
            cols = _chunk_cols(c)
            pair = _split_chunk(pot_ref[2 * c], pot_ref[2 * c + 1], half)
            weighted = weight * pair[m]
            term = weighted * moved_ref[m, :, cols].astype(jnp.float32)
            if tot_in_ref is None:
                tot_ref[m, :, cols] = term
            else:
                tot_ref[m, :, cols] = tot_in_ref[m, :, cols] + term
            pad_ref[PADC + c] = weighted * own_ref[m, :, cols].astype(jnp.float32)
            return carry

        lax.fori_loop(0, chunks, terms, 0)

        def gather(j, carry, m=m, wx=wx, wy=wy, wz=wz):
            cols = _chunk_cols(j)
            part = _shifted_chunk(pad_ref, j, -wx, -wy, -wz)
            if m == 0:
                acc_ref[:, cols] = part
            elif m + 1 < count:
                acc_ref[:, cols] = acc_ref[:, cols] + part
            else:
                back_ref[:, cols] = (acc_ref[:, cols] + part).astype(back_ref.dtype)
            return carry

        lax.fori_loop(0, chunks, gather, 0)


def shift_density(received, own, moves):
    rows, lanes = received.shape
    smem = pl.BlockSpec(memory_space=pltpu.SMEM)
    vmem = pl.BlockSpec(memory_space=pltpu.VMEM)
    return pl.pallas_call(
        _fwd_kernel,
        out_shape=(
            jax.ShapeDtypeStruct((rows, rows, 2 * rows), jnp.float32),
            jax.ShapeDtypeStruct(own.shape, jnp.bfloat16),
        ),
        in_specs=[smem, vmem, vmem],
        out_specs=(vmem, vmem),
        scratch_shapes=[
            pltpu.VMEM(own.shape, jnp.float32),
            pltpu.VMEM((lanes // 128 + 2 * PADC, rows, 128), jnp.float32),
        ],
    )(moves.reshape(-1), received, own)


def back_terms(moved, own, potential, totals, meta):
    _, rows, lanes = own.shape
    smem = pl.BlockSpec(memory_space=pltpu.SMEM)
    vmem = pl.BlockSpec(memory_space=pltpu.VMEM)
    operands = [meta, moved, own, potential]
    aliases = {}
    if totals is not None:
        operands.append(totals)
        aliases = {4: 0}
    return pl.pallas_call(
        _back_kernel,
        out_shape=(
            jax.ShapeDtypeStruct(own.shape, jnp.float32),
            jax.ShapeDtypeStruct((rows, lanes), jnp.bfloat16),
        ),
        in_specs=[smem] + [vmem] * (len(operands) - 1),
        out_specs=(vmem, vmem),
        scratch_shapes=[
            pltpu.VMEM((rows, lanes), jnp.float32),
            pltpu.VMEM((lanes // 128 + 2 * PADC, rows, 128), jnp.float32),
        ],
        input_output_aliases=aliases,
    )(*operands)


def solve_swapped(density, sine_matrix, depth_block, spectral):
    box_size = sine_matrix.shape[0]
    precise = lax.Precision.HIGH

    def along_z(field):
        return jnp.dot(
            field.reshape(box_size * box_size, 2 * box_size), depth_block,
            precision=precise, preferred_element_type=jnp.float32,
        ).reshape(box_size, box_size, 2 * box_size)

    def along_x(field):
        return jnp.einsum("ax,yxk->yak", sine_matrix, field, precision=precise,
                          preferred_element_type=jnp.float32)

    def along_y(field):
        return jnp.einsum("by,yxk->bxk", sine_matrix, field, precision=precise,
                          preferred_element_type=jnp.float32)

    field = along_y(along_x(along_z(density))) * spectral
    return along_z(along_x(along_y(field)))


def pick(table, index):
    hit = jnp.arange(table.shape[0], dtype=jnp.int32) == index
    hit = hit.reshape((table.shape[0],) + (1,) * (table.ndim - 1))
    return jnp.sum(jnp.where(hit, table, jnp.zeros_like(table)), axis=0)


def layer(orbitals, offsets, send_slot, pair_mask):
    owner_count = lax.axis_size(("orb", "grp"))
    far_stride = lax.axis_size("grp") * (lax.axis_size("orb") // 2 + 1)
    owner_index = lax.axis_index(("orb", "grp"))
    local_count = orbitals.shape[0]
    box_size = orbitals.shape[1]
    sine_matrix, eigenvalues = sine_table(box_size)
    depth_block = jnp.kron(jnp.eye(2, dtype=jnp.float32), sine_matrix)
    summed = eigenvalues[:, None, None] + eigenvalues[None, :, None] + eigenvalues[None, None, :]
    spectral_part = 1.0 / (summed + screening)
    spectral = jnp.concatenate((spectral_part, spectral_part), axis=2)
    members = jnp.arange(local_count, dtype=jnp.int32)
    own_offsets = jnp.stack(
        [pick(offsets, owner_index * local_count + m) for m in range(local_count)]
    )
    strides = []
    for round_index in range(ROUNDS):
        magnitude = 1 if round_index // 2 % 2 == 0 else far_stride
        strides.append(magnitude if round_index % 2 == 0 else -magnitude)
    my_slots = [pick(send_slot[r], owner_index) for r in range(ROUNDS)]
    sent_offsets = []
    for round_index in range(ROUNDS):
        sender = (owner_index - strides[round_index]) % owner_count
        sent_index = sender * local_count + pick(send_slot[round_index], sender)
        sent_offsets.append(pick(offsets, sent_index))
    move_table = own_offsets[None, :, :] - jnp.stack(sent_offsets)[:, None, :]
    totals = None
    arrived = {}
    for round_index in range(ROUNDS):
        outgoing = pick(orbitals, my_slots[round_index])
        arrived[round_index] = shifted(
            outgoing, ("orb", "grp"), strides[round_index] % owner_count
        )
    returned = {}
    for position, round_index in enumerate(ORDER):
        received = arrived[round_index]
        round_moves = move_table[round_index]
        density, moved = shift_density(received, orbitals, round_moves)
        potential = solve_swapped(density, sine_matrix, depth_block, spectral)
        meta = jnp.concatenate((round_moves.reshape(-1), pair_mask[round_index]))
        totals, back = back_terms(moved, orbitals, potential, totals, meta)
        if position + 1 < ROUNDS:
            nxt = ORDER[position + 1]
            back, arrived[nxt], totals = lax.optimization_barrier(
                (back, arrived[nxt], totals)
            )
        returned[round_index] = shifted(back, ("orb", "grp"), -strides[round_index] % owner_count)
    early = jnp.zeros_like(totals)
    for round_index in ORDER[:-1]:
        hit = (members == my_slots[round_index])[:, None, None]
        early = early + jnp.where(hit, returned[round_index].astype(jnp.float32)[None], 0.0)
    totals = totals + early
    totals = lax.optimization_barrier(totals)
    last = ORDER[-1]
    hit = (members == my_slots[last])[:, None, None]
    totals = totals + jnp.where(hit, returned[last].astype(jnp.float32)[None], 0.0)
    return totals


def solution(mesh):
    in_specs = (P(("orb", "grp"), None, None), P(), P(), P(None, ("orb", "grp")))
    out_specs = P(("orb", "grp"), None, None)
    return jax.shard_map(layer, mesh=mesh, in_specs=in_specs, out_specs=out_specs, check_vma=False)
```

```python
import math

import jax
import jax.numpy as jnp
from jax import lax
from jax.experimental import pallas as pl
from jax.experimental.pallas import tpu as pltpu
from jax.sharding import PartitionSpec as P


ROUNDS = 4


screening = 0.005


def shifted(value, axis, steps):
    count = lax.axis_size(axis)
    pairs = [(source, (source + steps) % count) for source in range(count)]
    return lax.ppermute(value, axis, pairs)


def sine_table(box_size):
    indices = jnp.arange(box_size, dtype=jnp.float32) + 1.0
    scaling = math.sqrt(2.0 / (box_size + 1))
    sine_matrix = scaling * jnp.sin(math.pi * jnp.outer(indices, indices) / (box_size + 1))
    eigenvalues = 2.0 - 2.0 * jnp.cos(math.pi * indices / (box_size + 1))
    return (sine_matrix, eigenvalues)


ORDER = (0, 2, 3, 1)

PADC = 9


def _chunk_cols(c):
    return pl.ds(pl.multiple_of(c * 128, 128), 128)


def _clear_pads(pad_ref):
    body = pad_ref.shape[0] - 2 * PADC
    zeros = jnp.zeros((PADC,) + pad_ref.shape[1:], jnp.float32)
    pad_ref[pl.ds(0, PADC)] = zeros
    pad_ref[pl.ds(PADC + body, PADC)] = zeros


def _shifted_chunk(pad_ref, j, wx, wy, wz):
    rows = pad_ref.shape[1]
    s = wy * rows + wz + 1024
    q = s // 128 - 8
    r = s % 128
    sh = (128 - r) % 128
    first = pltpu.roll(pad_ref[PADC + j + q], sh, 1)
    second = pltpu.roll(pad_ref[PADC + j + q + 1], sh, 1)
    lane = lax.broadcasted_iota(jnp.int32, (1, 128), 1)
    moved = jnp.where(lane < 128 - r, first, second)
    zz = lane % rows + wz
    yy = (j * 128 + lane) // rows + wy
    ok = (zz >= 0) & (zz < rows) & (yy >= 0) & (yy < rows)
    moved = pltpu.roll(moved, (rows - wx) % rows, 0)
    row = lax.broadcasted_iota(jnp.int32, (rows, 1), 0) + wx
    ok = ok & (row >= 0) & (row < rows)
    return jnp.where(ok, moved, 0.0)


def _join_chunk(first, second, half):
    even = jnp.where(half, first, pltpu.roll(second, 64, 1))
    odd = jnp.where(half, pltpu.roll(first, 64, 1), second)
    return even, odd


def _split_chunk(even, odd, half):
    first = jnp.where(half, even, pltpu.roll(odd, 64, 1))
    second = jnp.where(half, pltpu.roll(even, 64, 1), odd)
    return first, second


def _fwd_kernel(moves_ref, recv_ref, own_ref, dens_ref, moved_ref, work_ref, pad_ref):
    chunks = recv_ref.shape[1] // 128
    _clear_pads(pad_ref)

    def fill(c, carry):
        pad_ref[PADC + c] = recv_ref[:, _chunk_cols(c)].astype(jnp.float32)
        return carry

    lax.fori_loop(0, chunks, fill, 0, unroll=8)
    for m in range(own_ref.shape[0]):
        wx, wy, wz = moves_ref[3 * m], moves_ref[3 * m + 1], moves_ref[3 * m + 2]

        def shift(j, carry, m=m, wx=wx, wy=wy, wz=wz):
            cols = _chunk_cols(j)
            moved = _shifted_chunk(pad_ref, j, wx, wy, wz)
            moved_ref[m, :, cols] = moved.astype(moved_ref.dtype)
            work_ref[m, :, cols] = own_ref[m, :, cols].astype(jnp.float32) * moved
            return carry

        lax.fori_loop(0, chunks, shift, 0, unroll=8)
    half = lax.broadcasted_iota(jnp.int32, (1, 128), 1) < 64

    def body(c, carry):
        cols = _chunk_cols(c)
        even, odd = _join_chunk(work_ref[0, :, cols], work_ref[1, :, cols], half)
        dens_ref[2 * c] = even
        dens_ref[2 * c + 1] = odd
        return carry

    lax.fori_loop(0, dens_ref.shape[0] // 2, body, 0, unroll=8)


def _back_kernel(meta_ref, moved_ref, own_ref, pot_ref, *rest):
    if len(rest) == 5:
        tot_in_ref, tot_ref, back_ref, acc_ref, pad_ref = rest
    else:
        tot_in_ref = None
        tot_ref, back_ref, acc_ref, pad_ref = rest
    chunks = own_ref.shape[2] // 128
    half = lax.broadcasted_iota(jnp.int32, (1, 128), 1) < 64
    _clear_pads(pad_ref)
    count = own_ref.shape[0]
    for m in range(count):
        wx, wy, wz = meta_ref[3 * m], meta_ref[3 * m + 1], meta_ref[3 * m + 2]
        weight = meta_ref[6 + m].astype(jnp.float32)

        def terms(c, carry, m=m, weight=weight):
            cols = _chunk_cols(c)
            pair = _split_chunk(pot_ref[2 * c], pot_ref[2 * c + 1], half)
            weighted = weight * pair[m]
            term = weighted * moved_ref[m, :, cols].astype(jnp.float32)
            if tot_in_ref is None:
                tot_ref[m, :, cols] = term
            else:
                tot_ref[m, :, cols] = tot_in_ref[m, :, cols] + term
            pad_ref[PADC + c] = weighted * own_ref[m, :, cols].astype(jnp.float32)
            return carry

        lax.fori_loop(0, chunks, terms, 0, unroll=8)

        def gather(j, carry, m=m, wx=wx, wy=wy, wz=wz):
            cols = _chunk_cols(j)
            part = _shifted_chunk(pad_ref, j, -wx, -wy, -wz)
            if m == 0:
                acc_ref[:, cols] = part
            elif m + 1 < count:
                acc_ref[:, cols] = acc_ref[:, cols] + part
            else:
                back_ref[:, cols] = (acc_ref[:, cols] + part).astype(back_ref.dtype)
            return carry

        lax.fori_loop(0, chunks, gather, 0, unroll=8)


def shift_density(received, own, moves):
    rows, lanes = received.shape
    smem = pl.BlockSpec(memory_space=pltpu.SMEM)
    vmem = pl.BlockSpec(memory_space=pltpu.VMEM)
    return pl.pallas_call(
        _fwd_kernel,
        out_shape=(
            jax.ShapeDtypeStruct((rows, rows, 2 * rows), jnp.float32),
            jax.ShapeDtypeStruct(own.shape, jnp.bfloat16),
        ),
        in_specs=[smem, vmem, vmem],
        out_specs=(vmem, vmem),
        scratch_shapes=[
            pltpu.VMEM(own.shape, jnp.float32),
            pltpu.VMEM((lanes // 128 + 2 * PADC, rows, 128), jnp.float32),
        ],
    )(moves.reshape(-1), received, own)


def back_terms(moved, own, potential, totals, meta):
    _, rows, lanes = own.shape
    smem = pl.BlockSpec(memory_space=pltpu.SMEM)
    vmem = pl.BlockSpec(memory_space=pltpu.VMEM)
    operands = [meta, moved, own, potential]
    aliases = {}
    if totals is not None:
        operands.append(totals)
        aliases = {4: 0}
    return pl.pallas_call(
        _back_kernel,
        out_shape=(
            jax.ShapeDtypeStruct(own.shape, jnp.float32),
            jax.ShapeDtypeStruct((rows, lanes), jnp.bfloat16),
        ),
        in_specs=[smem] + [vmem] * (len(operands) - 1),
        out_specs=(vmem, vmem),
        scratch_shapes=[
            pltpu.VMEM((rows, lanes), jnp.float32),
            pltpu.VMEM((lanes // 128 + 2 * PADC, rows, 128), jnp.float32),
        ],
        input_output_aliases=aliases,
    )(*operands)


def solve_swapped(density, sine_matrix, depth_block, spectral):
    box_size = sine_matrix.shape[0]
    precise = lax.Precision.HIGH

    def along_z(field):
        return jnp.dot(
            field.reshape(box_size * box_size, 2 * box_size), depth_block,
            precision=precise, preferred_element_type=jnp.float32,
        ).reshape(box_size, box_size, 2 * box_size)

    def along_x(field):
        return jnp.einsum("ax,yxk->yak", sine_matrix, field, precision=precise,
                          preferred_element_type=jnp.float32)

    def along_y(field):
        return jnp.einsum("by,yxk->bxk", sine_matrix, field, precision=precise,
                          preferred_element_type=jnp.float32)

    field = along_y(along_x(along_z(density))) * spectral
    return along_z(along_x(along_y(field)))


def pick(table, index):
    hit = jnp.arange(table.shape[0], dtype=jnp.int32) == index
    hit = hit.reshape((table.shape[0],) + (1,) * (table.ndim - 1))
    return jnp.sum(jnp.where(hit, table, jnp.zeros_like(table)), axis=0)


def layer(orbitals, offsets, send_slot, pair_mask):
    owner_count = lax.axis_size(("orb", "grp"))
    far_stride = lax.axis_size("grp") * (lax.axis_size("orb") // 2 + 1)
    owner_index = lax.axis_index(("orb", "grp"))
    local_count = orbitals.shape[0]
    box_size = orbitals.shape[1]
    sine_matrix, eigenvalues = sine_table(box_size)
    depth_block = jnp.kron(jnp.eye(2, dtype=jnp.float32), sine_matrix)
    summed = eigenvalues[:, None, None] + eigenvalues[None, :, None] + eigenvalues[None, None, :]
    spectral_part = 1.0 / (summed + screening)
    spectral = jnp.concatenate((spectral_part, spectral_part), axis=2)
    members = jnp.arange(local_count, dtype=jnp.int32)
    own_offsets = jnp.stack(
        [pick(offsets, owner_index * local_count + m) for m in range(local_count)]
    )
    strides = []
    for round_index in range(ROUNDS):
        magnitude = 1 if round_index // 2 % 2 == 0 else far_stride
        strides.append(magnitude if round_index % 2 == 0 else -magnitude)
    my_slots = [pick(send_slot[r], owner_index) for r in range(ROUNDS)]
    sent_offsets = []
    for round_index in range(ROUNDS):
        sender = (owner_index - strides[round_index]) % owner_count
        sent_index = sender * local_count + pick(send_slot[round_index], sender)
        sent_offsets.append(pick(offsets, sent_index))
    move_table = own_offsets[None, :, :] - jnp.stack(sent_offsets)[:, None, :]
    totals = None
    arrived = {}
    for round_index in range(ROUNDS):
        outgoing = pick(orbitals, my_slots[round_index])
        arrived[round_index] = shifted(
            outgoing, ("orb", "grp"), strides[round_index] % owner_count
        )
    returned = {}
    for position, round_index in enumerate(ORDER):
        received = arrived[round_index]
        round_moves = move_table[round_index]
        density, moved = shift_density(received, orbitals, round_moves)
        potential = solve_swapped(density, sine_matrix, depth_block, spectral)
        meta = jnp.concatenate((round_moves.reshape(-1), pair_mask[round_index]))
        totals, back = back_terms(moved, orbitals, potential, totals, meta)
        if position + 1 < ROUNDS:
            nxt = ORDER[position + 1]
            back, arrived[nxt], totals = lax.optimization_barrier(
                (back, arrived[nxt], totals)
            )
        returned[round_index] = shifted(back, ("orb", "grp"), -strides[round_index] % owner_count)
    early = jnp.zeros_like(totals)
    for round_index in ORDER[:-1]:
        hit = (members == my_slots[round_index])[:, None, None]
        early = early + jnp.where(hit, returned[round_index].astype(jnp.float32)[None], 0.0)
    totals = totals + early
    totals = lax.optimization_barrier(totals)
    last = ORDER[-1]
    hit = (members == my_slots[last])[:, None, None]
    totals = totals + jnp.where(hit, returned[last].astype(jnp.float32)[None], 0.0)
    return totals


def solution(mesh):
    in_specs = (P(("orb", "grp"), None, None), P(), P(), P(None, ("orb", "grp")))
    out_specs = P(("orb", "grp"), None, None)
    return jax.shard_map(layer, mesh=mesh, in_specs=in_specs, out_specs=out_specs, check_vma=False)
```

```python
import math

import jax
import jax.numpy as jnp
from jax import lax
from jax.experimental import pallas as pl
from jax.experimental.pallas import tpu as pltpu
from jax.sharding import PartitionSpec as P


ROUNDS = 4


screening = 0.005


def shifted(value, axis, steps):
    count = lax.axis_size(axis)
    pairs = [(source, (source + steps) % count) for source in range(count)]
    return lax.ppermute(value, axis, pairs)


def sine_table(box_size):
    indices = jnp.arange(box_size, dtype=jnp.float32) + 1.0
    scaling = math.sqrt(2.0 / (box_size + 1))
    sine_matrix = scaling * jnp.sin(math.pi * jnp.outer(indices, indices) / (box_size + 1))
    eigenvalues = 2.0 - 2.0 * jnp.cos(math.pi * indices / (box_size + 1))
    return (sine_matrix, eigenvalues)


ORDER = (0, 2, 3, 1)


def _shift_one(x, wx, wy, wz):
    rows, lanes = x.shape
    s = wy * rows + wz
    r = pltpu.roll(x, (lanes - s) % lanes, 1).astype(jnp.float32)
    lane = lax.broadcasted_iota(jnp.int32, (1, lanes), 1)
    zz = lane % rows + wz
    yy = lane // rows + wy
    ok = (zz >= 0) & (zz < rows) & (yy >= 0) & (yy < rows)
    r = pltpu.roll(r, (rows - wx) % rows, 0)
    row = lax.broadcasted_iota(jnp.int32, (rows, 1), 0) + wx
    ok = ok & (row >= 0) & (row < rows)
    return jnp.where(ok, r, 0.0)


def _join_chunk(first, second, half):
    even = jnp.where(half, first, pltpu.roll(second, 64, 1))
    odd = jnp.where(half, pltpu.roll(first, 64, 1), second)
    return even, odd


def _split_chunk(even, odd, half):
    first = jnp.where(half, even, pltpu.roll(odd, 64, 1))
    second = jnp.where(half, pltpu.roll(even, 64, 1), odd)
    return first, second


def _fwd_kernel(moves_ref, recv_ref, own_ref, dens_ref, moved_ref, work_ref):
    x = recv_ref[...]
    for m in range(own_ref.shape[0]):
        moved = _shift_one(x, moves_ref[3 * m], moves_ref[3 * m + 1], moves_ref[3 * m + 2])
        moved_ref[m] = moved.astype(moved_ref.dtype)
        work_ref[m] = own_ref[m].astype(jnp.float32) * moved
    half = lax.broadcasted_iota(jnp.int32, (1, 128), 1) < 64

    def body(c, carry):
        cols = pl.ds(pl.multiple_of(c * 128, 128), 128)
        even, odd = _join_chunk(work_ref[0, :, cols], work_ref[1, :, cols], half)
        dens_ref[2 * c] = even
        dens_ref[2 * c + 1] = odd
        return carry

    lax.fori_loop(0, dens_ref.shape[0] // 2, body, 0, unroll=16)


def _back_kernel(meta_ref, moved_ref, own_ref, pot_ref, *rest):
    if len(rest) == 4:
        tot_in_ref, tot_ref, back_ref, work_ref = rest
    else:
        tot_in_ref = None
        tot_ref, back_ref, work_ref = rest
    half = lax.broadcasted_iota(jnp.int32, (1, 128), 1) < 64

    def body(c, carry):
        cols = pl.ds(pl.multiple_of(c * 128, 128), 128)
        first, second = _split_chunk(pot_ref[2 * c], pot_ref[2 * c + 1], half)
        work_ref[0, :, cols] = first
        work_ref[1, :, cols] = second
        return carry

    lax.fori_loop(0, pot_ref.shape[0] // 2, body, 0, unroll=16)
    acc = None
    for m in range(own_ref.shape[0]):
        wx, wy, wz = meta_ref[3 * m], meta_ref[3 * m + 1], meta_ref[3 * m + 2]
        weight = meta_ref[6 + m].astype(jnp.float32)
        weighted = weight * work_ref[m]
        term = weighted * moved_ref[m].astype(jnp.float32)
        tot_ref[m] = term if tot_in_ref is None else tot_in_ref[m] + term
        product = weighted * own_ref[m].astype(jnp.float32)
        part = _shift_one(product, -wx, -wy, -wz)
        acc = part if acc is None else acc + part
    back_ref[...] = acc.astype(back_ref.dtype)


def shift_density(received, own, moves):
    rows, _ = received.shape
    smem = pl.BlockSpec(memory_space=pltpu.SMEM)
    vmem = pl.BlockSpec(memory_space=pltpu.VMEM)
    return pl.pallas_call(
        _fwd_kernel,
        out_shape=(
            jax.ShapeDtypeStruct((rows, rows, 2 * rows), jnp.float32),
            jax.ShapeDtypeStruct(own.shape, jnp.bfloat16),
        ),
        in_specs=[smem, vmem, vmem],
        out_specs=(vmem, vmem),
        scratch_shapes=[pltpu.VMEM(own.shape, jnp.float32)],
    )(moves.reshape(-1), received, own)


def back_terms(moved, own, potential, totals, meta):
    _, rows, lanes = own.shape
    smem = pl.BlockSpec(memory_space=pltpu.SMEM)
    vmem = pl.BlockSpec(memory_space=pltpu.VMEM)
    operands = [meta, moved, own, potential]
    aliases = {}
    if totals is not None:
        operands.append(totals)
        aliases = {4: 0}
    return pl.pallas_call(
        _back_kernel,
        out_shape=(
            jax.ShapeDtypeStruct(own.shape, jnp.float32),
            jax.ShapeDtypeStruct((rows, lanes), jnp.bfloat16),
        ),
        in_specs=[smem] + [vmem] * (len(operands) - 1),
        out_specs=(vmem, vmem),
        scratch_shapes=[pltpu.VMEM(own.shape, jnp.float32)],
        input_output_aliases=aliases,
    )(*operands)


def solve_swapped(density, sine_matrix, depth_block, spectral):
    box_size = sine_matrix.shape[0]
    precise = lax.Precision.HIGH

    def along_z(field):
        return jnp.dot(
            field.reshape(box_size * box_size, 2 * box_size), depth_block,
            precision=precise, preferred_element_type=jnp.float32,
        ).reshape(box_size, box_size, 2 * box_size)

    def along_x(field):
        return jnp.einsum("ax,yxk->yak", sine_matrix, field, precision=precise,
                          preferred_element_type=jnp.float32)

    def along_y(field):
        return jnp.einsum("by,yxk->bxk", sine_matrix, field, precision=precise,
                          preferred_element_type=jnp.float32)

    field = along_y(along_x(along_z(density))) * spectral
    return along_z(along_x(along_y(field)))


def pick(table, index):
    hit = jnp.arange(table.shape[0], dtype=jnp.int32) == index
    hit = hit.reshape((table.shape[0],) + (1,) * (table.ndim - 1))
    return jnp.sum(jnp.where(hit, table, jnp.zeros_like(table)), axis=0)


def layer(orbitals, offsets, send_slot, pair_mask):
    owner_count = lax.axis_size(("orb", "grp"))
    far_stride = lax.axis_size("grp") * (lax.axis_size("orb") // 2 + 1)
    owner_index = lax.axis_index(("orb", "grp"))
    local_count = orbitals.shape[0]
    box_size = orbitals.shape[1]
    sine_matrix, eigenvalues = sine_table(box_size)
    depth_block = jnp.kron(jnp.eye(2, dtype=jnp.float32), sine_matrix)
    summed = eigenvalues[:, None, None] + eigenvalues[None, :, None] + eigenvalues[None, None, :]
    spectral_part = 1.0 / (summed + screening)
    spectral = jnp.concatenate((spectral_part, spectral_part), axis=2)
    members = jnp.arange(local_count, dtype=jnp.int32)
    own_offsets = jnp.stack(
        [pick(offsets, owner_index * local_count + m) for m in range(local_count)]
    )
    strides = []
    for round_index in range(ROUNDS):
        magnitude = 1 if round_index // 2 % 2 == 0 else far_stride
        strides.append(magnitude if round_index % 2 == 0 else -magnitude)
    my_slots = [pick(send_slot[r], owner_index) for r in range(ROUNDS)]
    sent_offsets = []
    for round_index in range(ROUNDS):
        sender = (owner_index - strides[round_index]) % owner_count
        sent_index = sender * local_count + pick(send_slot[round_index], sender)
        sent_offsets.append(pick(offsets, sent_index))
    move_table = own_offsets[None, :, :] - jnp.stack(sent_offsets)[:, None, :]
    totals = None
    arrived = {}
    for round_index in range(ROUNDS):
        outgoing = pick(orbitals, my_slots[round_index])
        arrived[round_index] = shifted(
            outgoing, ("orb", "grp"), strides[round_index] % owner_count
        )
    returned = {}
    for position, round_index in enumerate(ORDER):
        received = arrived[round_index]
        round_moves = move_table[round_index]
        density, moved = shift_density(received, orbitals, round_moves)
        potential = solve_swapped(density, sine_matrix, depth_block, spectral)
        meta = jnp.concatenate((round_moves.reshape(-1), pair_mask[round_index]))
        totals, back = back_terms(moved, orbitals, potential, totals, meta)
        if position + 1 < ROUNDS:
            nxt = ORDER[position + 1]
            back, arrived[nxt], totals = lax.optimization_barrier(
                (back, arrived[nxt], totals)
            )
        returned[round_index] = shifted(back, ("orb", "grp"), -strides[round_index] % owner_count)
    early = jnp.zeros_like(totals)
    for round_index in ORDER[:-1]:
        hit = (members == my_slots[round_index])[:, None, None]
        early = early + jnp.where(hit, returned[round_index].astype(jnp.float32)[None], 0.0)
    totals = totals + early
    totals = lax.optimization_barrier(totals)
    last = ORDER[-1]
    hit = (members == my_slots[last])[:, None, None]
    totals = totals + jnp.where(hit, returned[last].astype(jnp.float32)[None], 0.0)
    return totals


def solution(mesh):
    in_specs = (P(("orb", "grp"), None, None), P(), P(), P(None, ("orb", "grp")))
    out_specs = P(("orb", "grp"), None, None)
    return jax.shard_map(layer, mesh=mesh, in_specs=in_specs, out_specs=out_specs, check_vma=False)
```

```python
import math

import jax
import jax.numpy as jnp
from jax import lax
from jax.experimental import pallas as pl
from jax.experimental.pallas import tpu as pltpu
from jax.sharding import PartitionSpec as P


ROUNDS = 4


screening = 0.005


def shifted(value, axis, steps):
    count = lax.axis_size(axis)
    pairs = [(source, (source + steps) % count) for source in range(count)]
    return lax.ppermute(value, axis, pairs)


def sine_table(box_size):
    indices = jnp.arange(box_size, dtype=jnp.float32) + 1.0
    scaling = math.sqrt(2.0 / (box_size + 1))
    sine_matrix = scaling * jnp.sin(math.pi * jnp.outer(indices, indices) / (box_size + 1))
    eigenvalues = 2.0 - 2.0 * jnp.cos(math.pi * indices / (box_size + 1))
    return (sine_matrix, eigenvalues)


ORDER = (0, 2, 3, 1)

PADC = 9


def _chunk_cols(c):
    return pl.ds(pl.multiple_of(c * 128, 128), 128)


def _clear_pads(pad_ref):
    body = pad_ref.shape[0] - 2 * PADC
    zeros = jnp.zeros((PADC,) + pad_ref.shape[1:], jnp.float32)
    pad_ref[pl.ds(0, PADC)] = zeros
    pad_ref[pl.ds(PADC + body, PADC)] = zeros


def _shifted_chunk(pad_ref, j, wx, wy, wz):
    rows = pad_ref.shape[1]
    s = wy * rows + wz + 1024
    q = s // 128 - 8
    r = s % 128
    sh = (128 - r) % 128
    first = pltpu.roll(pad_ref[PADC + j + q], sh, 1)
    second = pltpu.roll(pad_ref[PADC + j + q + 1], sh, 1)
    lane = lax.broadcasted_iota(jnp.int32, (1, 128), 1)
    moved = jnp.where(lane < 128 - r, first, second)
    zz = lane % rows + wz
    yy = (j * 128 + lane) // rows + wy
    ok = (zz >= 0) & (zz < rows) & (yy >= 0) & (yy < rows)
    moved = pltpu.roll(moved, (rows - wx) % rows, 0)
    row = lax.broadcasted_iota(jnp.int32, (rows, 1), 0) + wx
    ok = ok & (row >= 0) & (row < rows)
    return jnp.where(ok, moved, 0.0)


def _shift_one(x, wx, wy, wz):
    rows, lanes = x.shape
    s = wy * rows + wz
    r = pltpu.roll(x, (lanes - s) % lanes, 1).astype(jnp.float32)
    lane = lax.broadcasted_iota(jnp.int32, (1, lanes), 1)
    zz = lane % rows + wz
    yy = lane // rows + wy
    ok = (zz >= 0) & (zz < rows) & (yy >= 0) & (yy < rows)
    r = pltpu.roll(r, (rows - wx) % rows, 0)
    row = lax.broadcasted_iota(jnp.int32, (rows, 1), 0) + wx
    ok = ok & (row >= 0) & (row < rows)
    return jnp.where(ok, r, 0.0)


def _join_chunk(first, second, half):
    even = jnp.where(half, first, pltpu.roll(second, 64, 1))
    odd = jnp.where(half, pltpu.roll(first, 64, 1), second)
    return even, odd


def _split_chunk(even, odd, half):
    first = jnp.where(half, even, pltpu.roll(odd, 64, 1))
    second = jnp.where(half, pltpu.roll(even, 64, 1), odd)
    return first, second


def _fwd_kernel(moves_ref, recv_ref, own_ref, dens_ref, moved_ref, work_ref, pad_ref):
    chunks = recv_ref.shape[1] // 128
    _clear_pads(pad_ref)

    def fill(c, carry):
        pad_ref[PADC + c] = recv_ref[:, _chunk_cols(c)].astype(jnp.float32)
        return carry

    lax.fori_loop(0, chunks, fill, 0, unroll=8)
    for m in range(own_ref.shape[0]):
        wx, wy, wz = moves_ref[3 * m], moves_ref[3 * m + 1], moves_ref[3 * m + 2]

        def shift(j, carry, m=m, wx=wx, wy=wy, wz=wz):
            cols = _chunk_cols(j)
            moved = _shifted_chunk(pad_ref, j, wx, wy, wz)
            moved_ref[m, :, cols] = moved.astype(moved_ref.dtype)
            work_ref[m, :, cols] = own_ref[m, :, cols].astype(jnp.float32) * moved
            return carry

        lax.fori_loop(0, chunks, shift, 0, unroll=8)
    half = lax.broadcasted_iota(jnp.int32, (1, 128), 1) < 64

    def body(c, carry):
        cols = _chunk_cols(c)
        even, odd = _join_chunk(work_ref[0, :, cols], work_ref[1, :, cols], half)
        dens_ref[2 * c] = even
        dens_ref[2 * c + 1] = odd
        return carry

    lax.fori_loop(0, dens_ref.shape[0] // 2, body, 0, unroll=8)


def _back_kernel(meta_ref, moved_ref, own_ref, pot_ref, *rest):
    if len(rest) == 4:
        tot_in_ref, tot_ref, back_ref, work_ref = rest
    else:
        tot_in_ref = None
        tot_ref, back_ref, work_ref = rest
    half = lax.broadcasted_iota(jnp.int32, (1, 128), 1) < 64

    def body(c, carry):
        cols = pl.ds(pl.multiple_of(c * 128, 128), 128)
        first, second = _split_chunk(pot_ref[2 * c], pot_ref[2 * c + 1], half)
        work_ref[0, :, cols] = first
        work_ref[1, :, cols] = second
        return carry

    lax.fori_loop(0, pot_ref.shape[0] // 2, body, 0, unroll=8)
    acc = None
    for m in range(own_ref.shape[0]):
        wx, wy, wz = meta_ref[3 * m], meta_ref[3 * m + 1], meta_ref[3 * m + 2]
        weight = meta_ref[6 + m].astype(jnp.float32)
        weighted = weight * work_ref[m]
        term = weighted * moved_ref[m].astype(jnp.float32)
        tot_ref[m] = term if tot_in_ref is None else tot_in_ref[m] + term
        product = weighted * own_ref[m].astype(jnp.float32)
        part = _shift_one(product, -wx, -wy, -wz)
        acc = part if acc is None else acc + part
    back_ref[...] = acc.astype(back_ref.dtype)


def shift_density(received, own, moves):
    rows, lanes = received.shape
    smem = pl.BlockSpec(memory_space=pltpu.SMEM)
    vmem = pl.BlockSpec(memory_space=pltpu.VMEM)
    return pl.pallas_call(
        _fwd_kernel,
        out_shape=(
            jax.ShapeDtypeStruct((rows, rows, 2 * rows), jnp.float32),
            jax.ShapeDtypeStruct(own.shape, jnp.bfloat16),
        ),
        in_specs=[smem, vmem, vmem],
        out_specs=(vmem, vmem),
        scratch_shapes=[
            pltpu.VMEM(own.shape, jnp.float32),
            pltpu.VMEM((lanes // 128 + 2 * PADC, rows, 128), jnp.float32),
        ],
    )(moves.reshape(-1), received, own)


def back_terms(moved, own, potential, totals, meta):
    _, rows, lanes = own.shape
    smem = pl.BlockSpec(memory_space=pltpu.SMEM)
    vmem = pl.BlockSpec(memory_space=pltpu.VMEM)
    operands = [meta, moved, own, potential]
    aliases = {}
    if totals is not None:
        operands.append(totals)
        aliases = {4: 0}
    return pl.pallas_call(
        _back_kernel,
        out_shape=(
            jax.ShapeDtypeStruct(own.shape, jnp.float32),
            jax.ShapeDtypeStruct((rows, lanes), jnp.bfloat16),
        ),
        in_specs=[smem] + [vmem] * (len(operands) - 1),
        out_specs=(vmem, vmem),
        scratch_shapes=[pltpu.VMEM(own.shape, jnp.float32)],
        input_output_aliases=aliases,
    )(*operands)


def solve_swapped(density, sine_matrix, depth_block, spectral):
    box_size = sine_matrix.shape[0]
    precise = lax.Precision.HIGH

    def along_z(field):
        return jnp.dot(
            field.reshape(box_size * box_size, 2 * box_size), depth_block,
            precision=precise, preferred_element_type=jnp.float32,
        ).reshape(box_size, box_size, 2 * box_size)

    def along_x(field):
        return jnp.einsum("ax,yxk->yak", sine_matrix, field, precision=precise,
                          preferred_element_type=jnp.float32)

    def along_y(field):
        return jnp.einsum("by,yxk->bxk", sine_matrix, field, precision=precise,
                          preferred_element_type=jnp.float32)

    field = along_y(along_x(along_z(density))) * spectral
    return along_z(along_x(along_y(field)))


def pick(table, index):
    hit = jnp.arange(table.shape[0], dtype=jnp.int32) == index
    hit = hit.reshape((table.shape[0],) + (1,) * (table.ndim - 1))
    return jnp.sum(jnp.where(hit, table, jnp.zeros_like(table)), axis=0)


def layer(orbitals, offsets, send_slot, pair_mask):
    owner_count = lax.axis_size(("orb", "grp"))
    far_stride = lax.axis_size("grp") * (lax.axis_size("orb") // 2 + 1)
    owner_index = lax.axis_index(("orb", "grp"))
    local_count = orbitals.shape[0]
    box_size = orbitals.shape[1]
    sine_matrix, eigenvalues = sine_table(box_size)
    depth_block = jnp.kron(jnp.eye(2, dtype=jnp.float32), sine_matrix)
    summed = eigenvalues[:, None, None] + eigenvalues[None, :, None] + eigenvalues[None, None, :]
    spectral_part = 1.0 / (summed + screening)
    spectral = jnp.concatenate((spectral_part, spectral_part), axis=2)
    members = jnp.arange(local_count, dtype=jnp.int32)
    own_offsets = jnp.stack(
        [pick(offsets, owner_index * local_count + m) for m in range(local_count)]
    )
    strides = []
    for round_index in range(ROUNDS):
        magnitude = 1 if round_index // 2 % 2 == 0 else far_stride
        strides.append(magnitude if round_index % 2 == 0 else -magnitude)
    my_slots = [pick(send_slot[r], owner_index) for r in range(ROUNDS)]
    sent_offsets = []
    for round_index in range(ROUNDS):
        sender = (owner_index - strides[round_index]) % owner_count
        sent_index = sender * local_count + pick(send_slot[round_index], sender)
        sent_offsets.append(pick(offsets, sent_index))
    move_table = own_offsets[None, :, :] - jnp.stack(sent_offsets)[:, None, :]
    totals = None
    arrived = {}
    for round_index in range(ROUNDS):
        outgoing = lax.select(my_slots[round_index] == 0, orbitals[0], orbitals[1])
        arrived[round_index] = shifted(
            outgoing, ("orb", "grp"), strides[round_index] % owner_count
        )
    returned = {}
    for position, round_index in enumerate(ORDER):
        received = arrived[round_index]
        round_moves = move_table[round_index]
        density, moved = shift_density(received, orbitals, round_moves)
        potential = solve_swapped(density, sine_matrix, depth_block, spectral)
        meta = jnp.concatenate((round_moves.reshape(-1), pair_mask[round_index]))
        totals, back = back_terms(moved, orbitals, potential, totals, meta)
        if position + 1 < ROUNDS:
            nxt = ORDER[position + 1]
            back, arrived[nxt], totals = lax.optimization_barrier(
                (back, arrived[nxt], totals)
            )
        returned[round_index] = shifted(back, ("orb", "grp"), -strides[round_index] % owner_count)
    early = jnp.zeros_like(totals)
    for round_index in ORDER[:-1]:
        hit = (members == my_slots[round_index])[:, None, None]
        early = early + jnp.where(hit, returned[round_index].astype(jnp.float32)[None], 0.0)
    totals = totals + early
    totals = lax.optimization_barrier(totals)
    last = ORDER[-1]
    hit = (members == my_slots[last])[:, None, None]
    totals = totals + jnp.where(hit, returned[last].astype(jnp.float32)[None], 0.0)
    return totals


def solution(mesh):
    in_specs = (P(("orb", "grp"), None, None), P(), P(), P(None, ("orb", "grp")))
    out_specs = P(("orb", "grp"), None, None)
    return jax.shard_map(layer, mesh=mesh, in_specs=in_specs, out_specs=out_specs, check_vma=False)
```
